256 devices in a mesh: feat: 8 (over x, core), rows: 32 (over y, z).
Axes of the slice: x: 4, y: 4, z: 8, core: 2. Of those that a mesh axis runs over, the one named last changes fastest.
Arguments:
- kernel: float32 [8192, 8192], P('rows', 'feat'), may hold values from -0.06629126 to 5, as said below
- train_feats: float32 [16384, 8192], P('rows', 'feat'), may hold values from -6 to 6
- test_feats: float32 [8192, 8192], P('rows', 'feat'), may hold values from -6 to 6
Outputs:
- factor_state: float32 [8192, 8192], P('rows', 'feat')
- train_state: float32 [16384, 8192], P('rows', 'feat')
- test_state: float32 [8192, 8192], P('rows', 'feat')
- scores: float32 [16384, 8192], P('rows', 'feat')
The draws below stay inside these ranges and needn't reach their ends.
Inputs may be any that keep to these rules, and one draw needn't show every extreme that they name: kernel is symmetric and positive definite; its diagonal dominates each row's other entries.
All inputs are finite; a program needn't handle non-finite values.
Results may differ from the reference program's by a relative error of at most 0.0001.
Values sent between devices are 32-bit elements; how exact they have to be, the bound alone decides.
No kernel may reach another device: no remote copies, remote signals or barrier semaphores. Data moves between devices by JAX's collectives and lax.ppermute only.
A program may use at most 128 MiB of HBM per device.

```python
import math
import jax
import jax.numpy as jnp
from jax import lax

F = 8192
PANEL = 256
NPAN = 2
TRAIN = 16384
TEST = 8192


def draw_kernel(key, part):
    entry_key, diagonal_key = jax.random.split(key)
    entries = jax.random.normal(entry_key, (F, F), jnp.float32)
    limit = 6.0 / math.sqrt(F)
    spread = jnp.clip((entries + entries.T) * (0.70710678 / math.sqrt(F)), -limit, limit)
    diagonal = jax.random.uniform(diagonal_key, (F,), jnp.float32, 3.0, 5.0)
    positions = jnp.arange(F)
    return jnp.where(positions[:, None] == positions[None, :], diagonal[:, None], spread)


def shard_levels(stream_key, dims, shards, smallest, high):
    level = 1.0
    for axis_at, blocks in shards:
        steps = jax.random.uniform(jax.random.fold_in(jax.random.fold_in(stream_key, 6), axis_at), (blocks,), jnp.float32, smallest / len(shards), high / len(shards))
        level = level * jnp.repeat(jnp.exp(steps), dims[axis_at] // blocks).reshape((-1,) + (1,) * (len(dims) - 1 - axis_at))
    return level


def scatter_about(stream_key, extent, deviation, most, pieces=(), kind=jnp.bfloat16):
    values = deviation * jax.random.normal(stream_key, extent, jnp.float32)
    if pieces:
        values = values * shard_levels(stream_key, extent, pieces, -0.22, 0.18)
    return jnp.clip(values, -most, most).astype(kind)


def setup_inputs(seed: int = 0) -> dict:
    splits = jax.random.split(jax.random.key(seed), 4)
    return {
        "kernel": draw_kernel(jax.random.fold_in(splits[3], 71), 0),
        "train_feats": scatter_about(splits[1], (TRAIN, F), 1.0, 6.0, ((0, 32), (1, 8)), jnp.float32),
        "test_feats": scatter_about(splits[2], (TEST, F), 1.0, 6.0, ((0, 32), (1, 8)), jnp.float32),
    }


def product(left, right):
    return jnp.dot(left.astype(jnp.float32), right.astype(jnp.float32), precision=lax.Precision.HIGHEST, preferred_element_type=jnp.float32)

def reference(kernel, train_feats, test_feats):
    matrix, train_work, test_work = (kernel, train_feats, test_feats)
    positions = jnp.arange(F)
    identity = jnp.eye(PANEL, dtype=jnp.float32)
    for panel in range(NPAN):
        first_col = panel * PANEL
        last_col = first_col + PANEL
        factor = jnp.linalg.cholesky(matrix[first_col:last_col, first_col:last_col])
        transposed = jax.scipy.linalg.solve_triangular(factor, identity, lower=True).T
        active = (positions >= first_col)[:, None]
        left_rows = jnp.where(active, product(matrix[:, first_col:last_col], transposed), 0.0)
        right_rows = jnp.where(active, product(matrix[first_col:last_col, :].T, transposed), 0.0)
        train_coords = product(train_work[:, first_col:last_col], transposed)
        test_coords = product(test_work[:, first_col:last_col], transposed)
        matrix = matrix - product(left_rows, right_rows.T)
        matrix = matrix.at[:, first_col:last_col].set(left_rows)
        train_work = train_work - product(train_coords, right_rows.T)
        train_work = train_work.at[:, first_col:last_col].set(train_coords)
        test_work = test_work - product(test_coords, right_rows.T)
        test_work = test_work.at[:, first_col:last_col].set(test_coords)
    coord_span = NPAN * PANEL
    upper = (positions[:, None] < coord_span) & (positions[None, :] >= coord_span)
    factor_state = jnp.where(upper, 0.0, matrix)
    scores = product(train_work[:, :coord_span], test_work[:, :coord_span].T)
    return (factor_state, train_work, test_work, scores)
```

```python
import jax
import jax.numpy as jnp
from jax import lax
from jax.sharding import PartitionSpec as P

PANEL = 256
NPAN = 2
CORES = 2
ZLEN = 8


def product(left, right):
    return jnp.dot(left, right, precision=lax.Precision.HIGHEST, preferred_element_type=jnp.float32)


def tree_offsets(sizes):
    strides = []
    for dim, size in enumerate(sizes):
        step = size // 2
        while step >= 1:
            strides.append((dim, step))
            step //= 2
    offsets = []
    for pos in range(2 ** len(strides)):
        off = [0] * len(sizes)
        for bit, (dim, step) in enumerate(strides):
            if (pos >> bit) & 1:
                off[dim] += step
        offsets.append(off)
    return offsets


def solution(mesh):
    names = tuple(mesh.axis_names)
    n_feat = mesh.shape["feat"]
    n_rows = mesh.shape["rows"]
    n_x = n_feat // CORES
    n_y = n_rows // ZLEN

    def lin(f, r):
        if names[0] == "feat":
            return f * n_rows + r
        return r * n_feat + f

    def dev(x, c, y, z):
        return lin((x % n_x) * CORES + (c % CORES), (y % n_y) * ZLEN + (z % ZLEN))

    def tree(value, me, groups):
        roots = jnp.array([g[0] for g in groups], jnp.int32)
        held = jnp.where(jnp.any(roots == me), value, jnp.zeros_like(value))
        step = 1
        while step < len(groups[0]):
            pairs = [(g[i], g[i + step]) for g in groups for i in range(step)]
            held = held + lax.ppermute(held, names, pairs)
            step *= 2
        return held

    feat_offsets = tree_offsets([n_x, CORES])
    all_offsets = tree_offsets([n_x, CORES, n_y, ZLEN])

    def whole_tree(root_r):
        y0, z0 = divmod(root_r, ZLEN)
        return [[dev(o[0], o[1], y0 + o[2], z0 + o[3]) for o in all_offsets]]

    def per_device(kernel, train_feats, test_feats):
        blk_rows, blk_cols = kernel.shape
        span = NPAN * PANEL
        row_index = lax.axis_index("rows")
        feat_index = lax.axis_index("feat")
        me = lin(feat_index, row_index)
        row_ids = row_index * blk_rows + jnp.arange(blk_rows, dtype=jnp.int32)
        col_ids = feat_index * blk_cols + jnp.arange(blk_cols, dtype=jnp.int32)
        identity = jnp.eye(PANEL, dtype=jnp.float32)

        diag0 = tree(kernel[:, :PANEL], me, whole_tree(0))
        diag1 = tree(kernel[:, :span], me, whole_tree(1))

        own = jnp.concatenate([kernel[:, :span], train_feats[:, :span], test_feats[:, :span]], axis=0)
        feat_groups = [[lin(o[0] * CORES + o[1], r) for o in feat_offsets] for r in range(n_rows)]
        own = tree(own, me, feat_groups)

        group = blk_cols // blk_rows
        pieces = n_rows // group
        piece_rows = blk_rows // pieces
        stacked = jnp.stack([kernel[:, :span], test_feats[:, :span]])
        piece = None
        for j in range(pieces):
            pairs = [(lin(0, r), lin(r // group, (r % group) * pieces + j)) for r in range(n_rows)]
            got = lax.ppermute(stacked[:, j * piece_rows:(j + 1) * piece_rows], names, pairs)
            piece = got if piece is None else piece + got
        column = lax.all_gather(piece, "rows", axis=1, tiled=True)

        factor0 = jnp.linalg.cholesky(diag0)
        first = jax.scipy.linalg.solve_triangular(factor0, identity, lower=True).T
        cross = product(diag1[:, :PANEL], first)
        factor1 = jnp.linalg.cholesky(diag1[:, PANEL:] - product(cross, cross.T))
        second = jax.scipy.linalg.solve_triangular(factor1, identity, lower=True).T

        def coords(block, ids=None):
            c0 = product(block[:, :PANEL], first)
            c1 = product(block[:, PANEL:] - product(c0, cross.T), second)
            if ids is not None:
                c1 = jnp.where((ids >= PANEL)[:, None], c1, 0.0)
            return jnp.concatenate([c0, c1], axis=1)

        left_rows = coords(own[:blk_rows], row_ids)
        train_rows = coords(own[blk_rows:blk_rows + train_feats.shape[0]])
        test_rows = coords(own[blk_rows + train_feats.shape[0]:])
        right_rows = coords(column[0], col_ids)
        test_cols = coords(column[1])

        in_panel = (col_ids < span)[None, :]
        pad = ((0, 0), (0, blk_cols - span))

        def finish(state, rows):
            updated = state - product(rows, right_rows.T)
            return jnp.where(in_panel, jnp.pad(rows, pad), updated)

        matrix = finish(kernel, left_rows)
        upper = (row_ids[:, None] < span) & (col_ids[None, :] >= span)
        matrix = jnp.where(upper, 0.0, matrix)
        train_work = finish(train_feats, train_rows)
        test_work = finish(test_feats, test_rows)
        scores = product(train_rows, test_cols.T)
        return (matrix, train_work, test_work, scores)

    return jax.shard_map(
        per_device,
        mesh=mesh,
        in_specs=(P("rows", "feat"), P("rows", "feat"), P("rows", "feat")),
        out_specs=(P("rows", "feat"), P("rows", "feat"), P("rows", "feat"), P("rows", "feat")),
        check_vma=False,
    )
```

```python
import jax
import jax.numpy as jnp
from jax import lax
from jax.sharding import PartitionSpec as P

PANEL = 256
NPAN = 2
CORES = 2
ZLEN = 8


def product(left, right):
    return jnp.dot(left, right, precision=lax.Precision.HIGHEST, preferred_element_type=jnp.float32)


def bulk_product(left, right):
    return jnp.dot(left, right, precision=lax.Precision.HIGH, preferred_element_type=jnp.float32)


def tree_offsets(sizes):
    strides = []
    for dim, size in enumerate(sizes):
        step = size // 2
        while step >= 1:
            strides.append((dim, step))
            step //= 2
    offsets = []
    for pos in range(2 ** len(strides)):
        off = [0] * len(sizes)
        for bit, (dim, step) in enumerate(strides):
            if (pos >> bit) & 1:
                off[dim] += step
        offsets.append(off)
    return offsets


def solution(mesh):
    names = tuple(mesh.axis_names)
    n_feat = mesh.shape["feat"]
    n_rows = mesh.shape["rows"]
    n_x = n_feat // CORES
    n_y = n_rows // ZLEN

    def lin(f, r):
        if names[0] == "feat":
            return f * n_rows + r
        return r * n_feat + f

    def dev(x, c, y, z):
        return lin((x % n_x) * CORES + (c % CORES), (y % n_y) * ZLEN + (z % ZLEN))

    def tree(value, me, groups):
        roots = jnp.array([g[0] for g in groups], jnp.int32)
        held = jnp.where(jnp.any(roots == me), value, jnp.zeros_like(value))
        step = 1
        while step < len(groups[0]):
            pairs = [(g[i], g[i + step]) for g in groups for i in range(step)]
            held = held + lax.ppermute(held, names, pairs)
            step *= 2
        return held

    feat_offsets = tree_offsets([n_x, CORES])
    all_offsets = tree_offsets([n_x, CORES, n_y, ZLEN])

    def whole_tree(root_r):
        y0, z0 = divmod(root_r, ZLEN)
        return [[dev(o[0], o[1], y0 + o[2], z0 + o[3]) for o in all_offsets]]

    def per_device(kernel, train_feats, test_feats):
        blk_rows, blk_cols = kernel.shape
        span = NPAN * PANEL
        row_index = lax.axis_index("rows")
        feat_index = lax.axis_index("feat")
        me = lin(feat_index, row_index)
        row_ids = row_index * blk_rows + jnp.arange(blk_rows, dtype=jnp.int32)
        col_ids = feat_index * blk_cols + jnp.arange(blk_cols, dtype=jnp.int32)
        identity = jnp.eye(PANEL, dtype=jnp.float32)

        diag0 = tree(kernel[:, :PANEL], me, whole_tree(0))
        diag0, kernel, train_feats, test_feats = lax.optimization_barrier(
            (diag0, kernel, train_feats, test_feats))
        diag1 = tree(kernel[:, :span], me, whole_tree(1))

        own = jnp.concatenate([kernel[:, :span], train_feats[:, :span], test_feats[:, :span]], axis=0)
        feat_groups = [[lin(o[0] * CORES + o[1], r) for o in feat_offsets] for r in range(n_rows)]
        own = tree(own, me, feat_groups)

        group = blk_cols // blk_rows
        pieces = n_rows // group
        piece_rows = blk_rows // pieces
        stacked = jnp.stack([kernel[:, :span], test_feats[:, :span]])
        piece = None
        for j in range(pieces):
            pairs = [(lin(0, r), lin(r // group, (r % group) * pieces + j)) for r in range(n_rows)]
            got = lax.ppermute(stacked[:, j * piece_rows:(j + 1) * piece_rows], names, pairs)
            piece = got if piece is None else piece + got
        column = lax.all_gather(piece, "rows", axis=1, tiled=True)

        factor0 = jnp.linalg.cholesky(diag0)
        first = jax.scipy.linalg.solve_triangular(factor0, identity, lower=True).T
        cross = product(diag1[:, :PANEL], first)
        factor1 = jnp.linalg.cholesky(diag1[:, PANEL:] - product(cross, cross.T))
        second = jax.scipy.linalg.solve_triangular(factor1, identity, lower=True).T

        def coords(block, ids=None):
            c0 = bulk_product(block[:, :PANEL], first)
            c1 = bulk_product(block[:, PANEL:] - bulk_product(c0, cross.T), second)
            if ids is not None:
                c1 = jnp.where((ids >= PANEL)[:, None], c1, 0.0)
            return jnp.concatenate([c0, c1], axis=1)

        left_rows = coords(own[:blk_rows], row_ids)
        train_rows = coords(own[blk_rows:blk_rows + train_feats.shape[0]])
        test_rows = coords(own[blk_rows + train_feats.shape[0]:])
        right_rows = coords(column[0], col_ids)
        test_cols = coords(column[1])

        in_panel = (col_ids < span)[None, :]
        pad = ((0, 0), (0, blk_cols - span))

        def finish(state, rows):
            updated = state - bulk_product(rows, right_rows.T)
            return jnp.where(in_panel, jnp.pad(rows, pad), updated)

        matrix = finish(kernel, left_rows)
        upper = (row_ids[:, None] < span) & (col_ids[None, :] >= span)
        matrix = jnp.where(upper, 0.0, matrix)
        train_work = finish(train_feats, train_rows)
        test_work = finish(test_feats, test_rows)
        scores = bulk_product(train_rows, test_cols.T)
        return (matrix, train_work, test_work, scores)

    return jax.shard_map(
        per_device,
        mesh=mesh,
        in_specs=(P("rows", "feat"), P("rows", "feat"), P("rows", "feat")),
        out_specs=(P("rows", "feat"), P("rows", "feat"), P("rows", "feat"), P("rows", "feat")),
        check_vma=False,
    )
```

```python
import jax
import jax.numpy as jnp
from jax import lax
from jax.sharding import PartitionSpec as P

PANEL = 256
NPAN = 2
CORES = 2
ZLEN = 8


def product(left, right):
    return jnp.dot(left, right, precision=lax.Precision.HIGHEST, preferred_element_type=jnp.float32)


def bulk_product(left, right):
    return jnp.dot(left, right, precision=lax.Precision.HIGHEST, preferred_element_type=jnp.float32)


def tree_offsets(sizes):
    strides = []
    for dim, size in enumerate(sizes):
        step = size // 2
        while step >= 1:
            strides.append((dim, step))
            step //= 2
    offsets = []
    for pos in range(2 ** len(strides)):
        off = [0] * len(sizes)
        for bit, (dim, step) in enumerate(strides):
            if (pos >> bit) & 1:
                off[dim] += step
        offsets.append(off)
    return offsets


def solution(mesh):
    names = tuple(mesh.axis_names)
    n_feat = mesh.shape["feat"]
    n_rows = mesh.shape["rows"]
    n_x = n_feat // CORES
    n_y = n_rows // ZLEN

    def lin(f, r):
        if names[0] == "feat":
            return f * n_rows + r
        return r * n_feat + f

    def dev(x, c, y, z):
        return lin((x % n_x) * CORES + (c % CORES), (y % n_y) * ZLEN + (z % ZLEN))

    def tree(value, me, groups):
        roots = jnp.array([g[0] for g in groups], jnp.int32)
        held = jnp.where(jnp.any(roots == me), value, jnp.zeros_like(value))
        step = 1
        while step < len(groups[0]):
            pairs = [(g[i], g[i + step]) for g in groups for i in range(step)]
            held = held + lax.ppermute(held, names, pairs)
            step *= 2
        return held

    feat_offsets = tree_offsets([n_x, CORES])
    all_offsets = tree_offsets([n_x, CORES, n_y, ZLEN])

    def whole_tree(root_r):
        y0, z0 = divmod(root_r, ZLEN)
        return [[dev(o[0], o[1], y0 + o[2], z0 + o[3]) for o in all_offsets]]

    def per_device(kernel, train_feats, test_feats):
        blk_rows, blk_cols = kernel.shape
        span = NPAN * PANEL
        row_index = lax.axis_index("rows")
        feat_index = lax.axis_index("feat")
        me = lin(feat_index, row_index)
        row_ids = row_index * blk_rows + jnp.arange(blk_rows, dtype=jnp.int32)
        col_ids = feat_index * blk_cols + jnp.arange(blk_cols, dtype=jnp.int32)
        identity = jnp.eye(PANEL, dtype=jnp.float32)

        diag0 = tree(kernel[:, :PANEL], me, whole_tree(0))
        diag1 = tree(kernel[:, :span], me, whole_tree(1))
        diag0, diag1, kernel, train_feats, test_feats = lax.optimization_barrier(
            (diag0, diag1, kernel, train_feats, test_feats))

        own = jnp.concatenate([kernel[:, :span], train_feats[:, :span], test_feats[:, :span]], axis=0)
        feat_groups = [[lin(o[0] * CORES + o[1], r) for o in feat_offsets] for r in range(n_rows)]
        own = tree(own, me, feat_groups)

        group = blk_cols // blk_rows
        pieces = n_rows // group
        piece_rows = blk_rows // pieces
        stacked = jnp.stack([kernel[:, :span], test_feats[:, :span]])
        piece = None
        for j in range(pieces):
            pairs = [(lin(0, r), lin(r // group, (r % group) * pieces + j)) for r in range(n_rows)]
            got = lax.ppermute(stacked[:, j * piece_rows:(j + 1) * piece_rows], names, pairs)
            piece = got if piece is None else piece + got
        column = lax.all_gather(piece, "rows", axis=1, tiled=True)

        factor0 = jnp.linalg.cholesky(diag0)
        first = jax.scipy.linalg.solve_triangular(factor0, identity, lower=True).T
        cross = product(diag1[:, :PANEL], first)
        factor1 = jnp.linalg.cholesky(diag1[:, PANEL:] - product(cross, cross.T))
        second = jax.scipy.linalg.solve_triangular(factor1, identity, lower=True).T

        def coords(block, ids=None):
            c0 = bulk_product(block[:, :PANEL], first)
            c1 = bulk_product(block[:, PANEL:] - bulk_product(c0, cross.T), second)
            if ids is not None:
                c1 = jnp.where((ids >= PANEL)[:, None], c1, 0.0)
            return jnp.concatenate([c0, c1], axis=1)

        left_rows = coords(own[:blk_rows], row_ids)
        train_rows = coords(own[blk_rows:blk_rows + train_feats.shape[0]])
        test_rows = coords(own[blk_rows + train_feats.shape[0]:])
        right_rows = coords(column[0], col_ids)
        test_cols = coords(column[1])

        in_panel = (col_ids < span)[None, :]
        pad = ((0, 0), (0, blk_cols - span))

        def finish(state, rows):
            updated = state - bulk_product(rows, right_rows.T)
            return jnp.where(in_panel, jnp.pad(rows, pad), updated)

        matrix = finish(kernel, left_rows)
        upper = (row_ids[:, None] < span) & (col_ids[None, :] >= span)
        matrix = jnp.where(upper, 0.0, matrix)
        train_work = finish(train_feats, train_rows)
        test_work = finish(test_feats, test_rows)
        scores = bulk_product(train_rows, test_cols.T)
        return (matrix, train_work, test_work, scores)

    return jax.shard_map(
        per_device,
        mesh=mesh,
        in_specs=(P("rows", "feat"), P("rows", "feat"), P("rows", "feat")),
        out_specs=(P("rows", "feat"), P("rows", "feat"), P("rows", "feat"), P("rows", "feat")),
        check_vma=False,
    )
```

```python
import jax
import jax.numpy as jnp
from jax import lax
from jax.sharding import PartitionSpec as P

PANEL = 256
NPAN = 2
CORES = 2
ZLEN = 8


def product(left, right):
    return jnp.dot(left, right, precision=lax.Precision.HIGHEST, preferred_element_type=jnp.float32)


def bulk_product(left, right):
    return jnp.dot(left, right, precision=lax.Precision.HIGHEST, preferred_element_type=jnp.float32)


def tree_offsets(sizes):
    strides = []
    for dim, size in enumerate(sizes):
        step = size // 2
        while step >= 1:
            strides.append((dim, step))
            step //= 2
    offsets = []
    for pos in range(2 ** len(strides)):
        off = [0] * len(sizes)
        for bit, (dim, step) in enumerate(strides):
            if (pos >> bit) & 1:
                off[dim] += step
        offsets.append(off)
    return offsets


def solution(mesh):
    names = tuple(mesh.axis_names)
    n_feat = mesh.shape["feat"]
    n_rows = mesh.shape["rows"]
    n_x = n_feat // CORES
    n_y = n_rows // ZLEN

    def lin(f, r):
        if names[0] == "feat":
            return f * n_rows + r
        return r * n_feat + f

    def dev(x, c, y, z):
        return lin((x % n_x) * CORES + (c % CORES), (y % n_y) * ZLEN + (z % ZLEN))

    def tree(value, me, groups):
        roots = jnp.array([g[0] for g in groups], jnp.int32)
        held = jnp.where(jnp.any(roots == me), value, jnp.zeros_like(value))
        step = 1
        while step < len(groups[0]):
            pairs = [(g[i], g[i + step]) for g in groups for i in range(step)]
            held = held + lax.ppermute(held, names, pairs)
            step *= 2
        return held

    feat_offsets = tree_offsets([n_x, CORES])
    all_offsets = tree_offsets([n_x, CORES, n_y, ZLEN])

    def whole_tree(root_r):
        y0, z0 = divmod(root_r, ZLEN)
        return [[dev(o[0], o[1], y0 + o[2], z0 + o[3]) for o in all_offsets]]

    def per_device(kernel, train_feats, test_feats):
        blk_rows, blk_cols = kernel.shape
        span = NPAN * PANEL
        row_index = lax.axis_index("rows")
        feat_index = lax.axis_index("feat")
        me = lin(feat_index, row_index)
        row_ids = row_index * blk_rows + jnp.arange(blk_rows, dtype=jnp.int32)
        col_ids = feat_index * blk_cols + jnp.arange(blk_cols, dtype=jnp.int32)
        identity = jnp.eye(PANEL, dtype=jnp.float32)

        diag1 = lax.ppermute(kernel[:, :span], names, [(lin(0, 1), lin(0, 0))])

        own = jnp.concatenate([kernel[:, :span], train_feats[:, :span], test_feats[:, :span]], axis=0)
        feat_groups = [[lin(o[0] * CORES + o[1], r) for o in feat_offsets] for r in range(n_rows)]
        own = tree(own, me, feat_groups)

        group = blk_cols // blk_rows
        pieces = n_rows // group
        piece_rows = blk_rows // pieces
        stacked = jnp.stack([kernel[:, :span], test_feats[:, :span]])
        piece = None
        for j in range(pieces):
            pairs = [(lin(0, r), lin(r // group, (r % group) * pieces + j)) for r in range(n_rows)]
            got = lax.ppermute(stacked[:, j * piece_rows:(j + 1) * piece_rows], names, pairs)
            piece = got if piece is None else piece + got
        column = lax.all_gather(piece, "rows", axis=1, tiled=True)

        factor0 = jnp.linalg.cholesky(kernel[:, :PANEL])
        first = jax.scipy.linalg.solve_triangular(factor0, identity, lower=True).T
        cross = product(diag1[:, :PANEL], first)
        factor1 = jnp.linalg.cholesky(diag1[:, PANEL:] - product(cross, cross.T))
        second = jax.scipy.linalg.solve_triangular(factor1, identity, lower=True).T
        held = tree(jnp.concatenate([first, cross], axis=1), me, whole_tree(0))
        first, cross = held[:, :PANEL], held[:, PANEL:]
        second = tree(second, me, whole_tree(0))

        def coords(block, ids=None):
            c0 = bulk_product(block[:, :PANEL], first)
            c1 = bulk_product(block[:, PANEL:] - bulk_product(c0, cross.T), second)
            if ids is not None:
                c1 = jnp.where((ids >= PANEL)[:, None], c1, 0.0)
            return jnp.concatenate([c0, c1], axis=1)

        left_rows = coords(own[:blk_rows], row_ids)
        train_rows = coords(own[blk_rows:blk_rows + train_feats.shape[0]])
        test_rows = coords(own[blk_rows + train_feats.shape[0]:])
        right_rows = coords(column[0], col_ids)
        test_cols = coords(column[1])

        in_panel = (col_ids < span)[None, :]
        pad = ((0, 0), (0, blk_cols - span))

        def finish(state, rows):
            updated = state - bulk_product(rows, right_rows.T)
            return jnp.where(in_panel, jnp.pad(rows, pad), updated)

        matrix = finish(kernel, left_rows)
        upper = (row_ids[:, None] < span) & (col_ids[None, :] >= span)
        matrix = jnp.where(upper, 0.0, matrix)
        train_work = finish(train_feats, train_rows)
        test_work = finish(test_feats, test_rows)
        scores = bulk_product(train_rows, test_cols.T)
        return (matrix, train_work, test_work, scores)

    return jax.shard_map(
        per_device,
        mesh=mesh,
        in_specs=(P("rows", "feat"), P("rows", "feat"), P("rows", "feat")),
        out_specs=(P("rows", "feat"), P("rows", "feat"), P("rows", "feat"), P("rows", "feat")),
        check_vma=False,
    )
```

```python
import jax
import jax.numpy as jnp
from jax import lax
from jax.sharding import PartitionSpec as P

PANEL = 256
NPAN = 2
CORES = 2
ZLEN = 8


def product(left, right):
    return jnp.dot(left, right, precision=lax.Precision.HIGHEST, preferred_element_type=jnp.float32)


def bulk_product(left, right):
    return jnp.dot(left, right, precision=lax.Precision.HIGHEST, preferred_element_type=jnp.float32)


def tree_offsets(sizes):
    strides = []
    for dim, size in enumerate(sizes):
        step = size // 2
        while step >= 1:
            strides.append((dim, step))
            step //= 2
    offsets = []
    for pos in range(2 ** len(strides)):
        off = [0] * len(sizes)
        for bit, (dim, step) in enumerate(strides):
            if (pos >> bit) & 1:
                off[dim] += step
        offsets.append(off)
    return offsets


def solution(mesh):
    names = tuple(mesh.axis_names)
    n_feat = mesh.shape["feat"]
    n_rows = mesh.shape["rows"]
    n_x = n_feat // CORES
    n_y = n_rows // ZLEN

    def lin(f, r):
        if names[0] == "feat":
            return f * n_rows + r
        return r * n_feat + f

    def dev(x, c, y, z):
        return lin((x % n_x) * CORES + (c % CORES), (y % n_y) * ZLEN + (z % ZLEN))

    def tree(value, me, groups):
        roots = jnp.array([g[0] for g in groups], jnp.int32)
        held = jnp.where(jnp.any(roots == me), value, jnp.zeros_like(value))
        step = 1
        while step < len(groups[0]):
            pairs = [(g[i], g[i + step]) for g in groups for i in range(step)]
            held = held + lax.ppermute(held, names, pairs)
            step *= 2
        return held

    feat_offsets = tree_offsets([n_x, CORES])
    all_offsets = tree_offsets([n_x, CORES, n_y, ZLEN])

    def whole_tree(root_r):
        y0, z0 = divmod(root_r, ZLEN)
        return [[dev(o[0], o[1], y0 + o[2], z0 + o[3]) for o in all_offsets]]

    def per_device(kernel, train_feats, test_feats):
        blk_rows, blk_cols = kernel.shape
        span = NPAN * PANEL
        row_index = lax.axis_index("rows")
        feat_index = lax.axis_index("feat")
        me = lin(feat_index, row_index)
        row_ids = row_index * blk_rows + jnp.arange(blk_rows, dtype=jnp.int32)
        col_ids = feat_index * blk_cols + jnp.arange(blk_cols, dtype=jnp.int32)
        identity = jnp.eye(PANEL, dtype=jnp.float32)

        diag1 = lax.ppermute(kernel[:, :span], names, [(lin(0, 1), lin(0, 0))])

        group = blk_cols // blk_rows
        pieces = n_rows // group
        piece_rows = blk_rows // pieces
        stacked = jnp.stack([kernel[:, :span], test_feats[:, :span]])
        piece = None
        for j in range(pieces):
            pairs = [(lin(0, r), lin(r // group, (r % group) * pieces + j)) for r in range(n_rows)]
            got = lax.ppermute(stacked[:, j * piece_rows:(j + 1) * piece_rows], names, pairs)
            piece = got if piece is None else piece + got
        column = lax.all_gather(piece, "rows", axis=1, tiled=True)
        piece, kernel, train_feats, test_feats = lax.optimization_barrier(
            (piece, kernel, train_feats, test_feats))
        own = jnp.concatenate([kernel[:, :span], train_feats[:, :span], test_feats[:, :span]], axis=0)
        feat_groups = [[lin(o[0] * CORES + o[1], r) for o in feat_offsets] for r in range(n_rows)]
        own = tree(own, me, feat_groups)

        factor0 = jnp.linalg.cholesky(kernel[:, :PANEL])
        first = jax.scipy.linalg.solve_triangular(factor0, identity, lower=True).T
        cross = product(diag1[:, :PANEL], first)
        factor1 = jnp.linalg.cholesky(diag1[:, PANEL:] - product(cross, cross.T))
        second = jax.scipy.linalg.solve_triangular(factor1, identity, lower=True).T
        held = tree(jnp.concatenate([first, cross, second], axis=1), me, whole_tree(0))
        first, cross, second = held[:, :PANEL], held[:, PANEL:2 * PANEL], held[:, 2 * PANEL:]

        def coords(block, ids=None):
            c0 = bulk_product(block[:, :PANEL], first)
            c1 = bulk_product(block[:, PANEL:] - bulk_product(c0, cross.T), second)
            if ids is not None:
                c1 = jnp.where((ids >= PANEL)[:, None], c1, 0.0)
            return jnp.concatenate([c0, c1], axis=1)

        left_rows = coords(own[:blk_rows], row_ids)
        train_rows = coords(own[blk_rows:blk_rows + train_feats.shape[0]])
        test_rows = coords(own[blk_rows + train_feats.shape[0]:])
        right_rows = coords(column[0], col_ids)
        test_cols = coords(column[1])

        in_panel = (col_ids < span)[None, :]
        pad = ((0, 0), (0, blk_cols - span))

        def finish(state, rows):
            updated = state - bulk_product(rows, right_rows.T)
            return jnp.where(in_panel, jnp.pad(rows, pad), updated)

        matrix = finish(kernel, left_rows)
        upper = (row_ids[:, None] < span) & (col_ids[None, :] >= span)
        matrix = jnp.where(upper, 0.0, matrix)
        train_work = finish(train_feats, train_rows)
        test_work = finish(test_feats, test_rows)
        scores = bulk_product(train_rows, test_cols.T)
        return (matrix, train_work, test_work, scores)

    return jax.shard_map(
        per_device,
        mesh=mesh,
        in_specs=(P("rows", "feat"), P("rows", "feat"), P("rows", "feat")),
        out_specs=(P("rows", "feat"), P("rows", "feat"), P("rows", "feat"), P("rows", "feat")),
        check_vma=False,
    )
```

```python
import jax
import jax.numpy as jnp
from jax import lax
from jax.sharding import PartitionSpec as P

PANEL = 256
NPAN = 2
CORES = 2
ZLEN = 8


def product(left, right):
    return jnp.dot(left, right, precision=lax.Precision.HIGHEST, preferred_element_type=jnp.float32)


def bulk_product(left, right):
    return jnp.dot(left, right, precision=lax.Precision.HIGHEST, preferred_element_type=jnp.float32)


def tree_offsets(sizes):
    strides = []
    for dim, size in enumerate(sizes):
        step = size // 2
        while step >= 1:
            strides.append((dim, step))
            step //= 2
    offsets = []
    for pos in range(2 ** len(strides)):
        off = [0] * len(sizes)
        for bit, (dim, step) in enumerate(strides):
            if (pos >> bit) & 1:
                off[dim] += step
        offsets.append(off)
    return offsets


def solution(mesh):
    names = tuple(mesh.axis_names)
    n_feat = mesh.shape["feat"]
    n_rows = mesh.shape["rows"]
    n_x = n_feat // CORES
    n_y = n_rows // ZLEN

    def lin(f, r):
        if names[0] == "feat":
            return f * n_rows + r
        return r * n_feat + f

    def dev(x, c, y, z):
        return lin((x % n_x) * CORES + (c % CORES), (y % n_y) * ZLEN + (z % ZLEN))

    def tree(value, me, groups):
        roots = jnp.array([g[0] for g in groups], jnp.int32)
        held = jnp.where(jnp.any(roots == me), value, jnp.zeros_like(value))
        step = 1
        while step < len(groups[0]):
            pairs = [(g[i], g[i + step]) for g in groups for i in range(step)]
            held = held + lax.ppermute(held, names, pairs)
            step *= 2
        return held

    feat_offsets = tree_offsets([n_x, CORES])
    all_offsets = tree_offsets([n_y, ZLEN, n_x, CORES])

    def whole_tree(root_r):
        y0, z0 = divmod(root_r, ZLEN)
        return [[dev(o[2], o[3], y0 + o[0], z0 + o[1]) for o in all_offsets]]

    def per_device(kernel, train_feats, test_feats):
        blk_rows, blk_cols = kernel.shape
        span = NPAN * PANEL
        row_index = lax.axis_index("rows")
        feat_index = lax.axis_index("feat")
        me = lin(feat_index, row_index)
        row_ids = row_index * blk_rows + jnp.arange(blk_rows, dtype=jnp.int32)
        col_ids = feat_index * blk_cols + jnp.arange(blk_cols, dtype=jnp.int32)
        identity = jnp.eye(PANEL, dtype=jnp.float32)

        own = jnp.concatenate([kernel[:, :span], train_feats[:, :span], test_feats[:, :span]], axis=0)
        feat_groups = [[lin(o[0] * CORES + o[1], r) for o in feat_offsets] for r in range(n_rows)]
        own = tree(own, me, feat_groups)

        diag0 = tree(kernel[:, :PANEL], me, whole_tree(0))
        diag1 = tree(kernel[:, :span], me, whole_tree(1))
        diag0, diag1, kernel, train_feats, test_feats = lax.optimization_barrier(
            (diag0, diag1, kernel, train_feats, test_feats))

        group = blk_cols // blk_rows
        pieces = n_rows // group
        piece_rows = blk_rows // pieces
        stacked = jnp.stack([kernel[:, :span], test_feats[:, :span]])
        piece = None
        for j in range(pieces):
            pairs = [(lin(0, r), lin(r // group, (r % group) * pieces + j)) for r in range(n_rows)]
            got = lax.ppermute(stacked[:, j * piece_rows:(j + 1) * piece_rows], names, pairs)
            piece = got if piece is None else piece + got
        column = lax.all_gather(piece, "rows", axis=1, tiled=True)

        factor0 = jnp.linalg.cholesky(diag0)
        first = jax.scipy.linalg.solve_triangular(factor0, identity, lower=True).T
        cross = product(diag1[:, :PANEL], first)
        factor1 = jnp.linalg.cholesky(diag1[:, PANEL:] - product(cross, cross.T))
        second = jax.scipy.linalg.solve_triangular(factor1, identity, lower=True).T

        def coords(block, ids=None):
            c0 = bulk_product(block[:, :PANEL], first)
            c1 = bulk_product(block[:, PANEL:] - bulk_product(c0, cross.T), second)
            if ids is not None:
                c1 = jnp.where((ids >= PANEL)[:, None], c1, 0.0)
            return jnp.concatenate([c0, c1], axis=1)

        left_rows = coords(own[:blk_rows], row_ids)
        train_rows = coords(own[blk_rows:blk_rows + train_feats.shape[0]])
        test_rows = coords(own[blk_rows + train_feats.shape[0]:])
        right_rows = coords(column[0], col_ids)
        test_cols = coords(column[1])

        in_panel = (col_ids < span)[None, :]
        pad = ((0, 0), (0, blk_cols - span))

        def finish(state, rows):
            updated = state - bulk_product(rows, right_rows.T)
            return jnp.where(in_panel, jnp.pad(rows, pad), updated)

        matrix = finish(kernel, left_rows)
        upper = (row_ids[:, None] < span) & (col_ids[None, :] >= span)
        matrix = jnp.where(upper, 0.0, matrix)
        train_work = finish(train_feats, train_rows)
        test_work = finish(test_feats, test_rows)
        scores = bulk_product(train_rows, test_cols.T)
        return (matrix, train_work, test_work, scores)

    return jax.shard_map(
        per_device,
        mesh=mesh,
        in_specs=(P("rows", "feat"), P("rows", "feat"), P("rows", "feat")),
        out_specs=(P("rows", "feat"), P("rows", "feat"), P("rows", "feat"), P("rows", "feat")),
        check_vma=False,
    )
```

```python
import numpy as np
import jax
import jax.numpy as jnp
from jax import lax
from jax.sharding import PartitionSpec as P

PANEL = 256
NPAN = 2
CORES = 2
ZLEN = 8


def product(left, right):
    return jnp.dot(left, right, precision=lax.Precision.HIGHEST, preferred_element_type=jnp.float32)


def bulk_product(left, right):
    return jnp.dot(left, right, precision=lax.Precision.HIGHEST, preferred_element_type=jnp.float32)


def tree_offsets(sizes):
    strides = []
    for dim, size in enumerate(sizes):
        step = size // 2
        while step >= 1:
            strides.append((dim, step))
            step //= 2
    offsets = []
    for pos in range(2 ** len(strides)):
        off = [0] * len(sizes)
        for bit, (dim, step) in enumerate(strides):
            if (pos >> bit) & 1:
                off[dim] += step
        offsets.append(off)
    return offsets


def solution(mesh):
    names = tuple(mesh.axis_names)
    n_feat = mesh.shape["feat"]
    n_rows = mesh.shape["rows"]
    n_x = n_feat // CORES
    n_y = n_rows // ZLEN

    def lin(f, r):
        if names[0] == "feat":
            return f * n_rows + r
        return r * n_feat + f

    def dev(x, c, y, z):
        return lin((x % n_x) * CORES + (c % CORES), (y % n_y) * ZLEN + (z % ZLEN))

    def tree(value, me, groups):
        roots = jnp.array([g[0] for g in groups], jnp.int32)
        held = jnp.where(jnp.any(roots == me), value, jnp.zeros_like(value))
        step = 1
        while step < len(groups[0]):
            pairs = [(g[i], g[i + step]) for g in groups for i in range(step)]
            held = held + lax.ppermute(held, names, pairs)
            step *= 2
        return held

    feat_offsets = tree_offsets([n_x, CORES])
    all_offsets = tree_offsets([n_y, ZLEN, n_x, CORES])

    row_offsets = tree_offsets([n_y, ZLEN])

    def row_dev(root_r, off):
        y0, z0 = divmod(root_r, ZLEN)
        return lin(0, ((y0 + off[0]) % n_y) * ZLEN + (z0 + off[1]) % ZLEN)

    def diag_trees(block, me, feat_groups):
        held0 = jnp.where(me == row_dev(0, [0, 0]), block, jnp.zeros_like(block))
        held1 = jnp.where(me == row_dev(1, [0, 0]), block, jnp.zeros_like(block))
        step = 1
        while step < len(row_offsets):
            pairs0 = [(row_dev(0, row_offsets[i]), row_dev(0, row_offsets[i + step])) for i in range(step)]
            pairs1 = [(row_dev(1, row_offsets[i]), row_dev(1, row_offsets[i + step])) for i in range(step)]
            pairs = pairs0 + pairs1
            assert len({a for a, _ in pairs}) == len(pairs) and len({b for _, b in pairs}) == len(pairs)
            got = lax.ppermute(held0 + held1, names, pairs)
            table = np.zeros(n_feat * n_rows, bool)
            table[[b for _, b in pairs0]] = True
            to0 = jnp.asarray(table)[me]
            held0 = held0 + jnp.where(to0, got, 0.0)
            held1 = held1 + jnp.where(to0, 0.0, got)
            step *= 2
        both = tree(jnp.concatenate([held0[:, :PANEL], held1], axis=1), me, feat_groups)
        return both[:, :PANEL], both[:, PANEL:]

    def whole_tree(root_r):
        y0, z0 = divmod(root_r, ZLEN)
        return [[dev(o[2], o[3], y0 + o[0], z0 + o[1]) for o in all_offsets]]

    def per_device(kernel, train_feats, test_feats):
        blk_rows, blk_cols = kernel.shape
        span = NPAN * PANEL
        row_index = lax.axis_index("rows")
        feat_index = lax.axis_index("feat")
        me = lin(feat_index, row_index)
        row_ids = row_index * blk_rows + jnp.arange(blk_rows, dtype=jnp.int32)
        col_ids = feat_index * blk_cols + jnp.arange(blk_cols, dtype=jnp.int32)
        identity = jnp.eye(PANEL, dtype=jnp.float32)

        own = jnp.concatenate([kernel[:, :span], train_feats[:, :span], test_feats[:, :span]], axis=0)
        feat_groups = [[lin(o[0] * CORES + o[1], r) for o in feat_offsets] for r in range(n_rows)]
        own = tree(own, me, feat_groups)

        diag0, diag1 = diag_trees(kernel[:, :span], me, feat_groups)
        diag0, diag1, kernel, train_feats, test_feats = lax.optimization_barrier(
            (diag0, diag1, kernel, train_feats, test_feats))

        group = blk_cols // blk_rows
        pieces = n_rows // group
        piece_rows = blk_rows // pieces
        stacked = jnp.stack([kernel[:, :span], test_feats[:, :span]])
        piece = None
        for j in range(pieces):
            pairs = [(lin(0, r), lin(r // group, (r % group) * pieces + j)) for r in range(n_rows)]
            got = lax.ppermute(stacked[:, j * piece_rows:(j + 1) * piece_rows], names, pairs)
            piece = got if piece is None else piece + got
        column = lax.all_gather(piece, "rows", axis=1, tiled=True)

        factor0 = jnp.linalg.cholesky(diag0)
        first = jax.scipy.linalg.solve_triangular(factor0, identity, lower=True).T
        cross = product(diag1[:, :PANEL], first)
        factor1 = jnp.linalg.cholesky(diag1[:, PANEL:] - product(cross, cross.T))
        second = jax.scipy.linalg.solve_triangular(factor1, identity, lower=True).T

        def coords(block, ids=None):
            c0 = bulk_product(block[:, :PANEL], first)
            c1 = bulk_product(block[:, PANEL:] - bulk_product(c0, cross.T), second)
            if ids is not None:
                c1 = jnp.where((ids >= PANEL)[:, None], c1, 0.0)
            return jnp.concatenate([c0, c1], axis=1)

        left_rows = coords(own[:blk_rows], row_ids)
        train_rows = coords(own[blk_rows:blk_rows + train_feats.shape[0]])
        test_rows = coords(own[blk_rows + train_feats.shape[0]:])
        right_rows = coords(column[0], col_ids)
        test_cols = coords(column[1])

        in_panel = (col_ids < span)[None, :]
        pad = ((0, 0), (0, blk_cols - span))

        def finish(state, rows):
            updated = state - bulk_product(rows, right_rows.T)
            return jnp.where(in_panel, jnp.pad(rows, pad), updated)

        matrix = finish(kernel, left_rows)
        upper = (row_ids[:, None] < span) & (col_ids[None, :] >= span)
        matrix = jnp.where(upper, 0.0, matrix)
        train_work = finish(train_feats, train_rows)
        test_work = finish(test_feats, test_rows)
        scores = bulk_product(train_rows, test_cols.T)
        return (matrix, train_work, test_work, scores)

    return jax.shard_map(
        per_device,
        mesh=mesh,
        in_specs=(P("rows", "feat"), P("rows", "feat"), P("rows", "feat")),
        out_specs=(P("rows", "feat"), P("rows", "feat"), P("rows", "feat"), P("rows", "feat")),
        check_vma=False,
    )
```

```python
import jax
import jax.numpy as jnp
from jax import lax
from jax.sharding import PartitionSpec as P

PANEL = 256
NPAN = 2
CORES = 2
ZLEN = 8


def product(left, right):
    return jnp.dot(left, right, precision=lax.Precision.HIGHEST, preferred_element_type=jnp.float32)


def bulk_product(left, right):
    return jnp.dot(left, right, precision=lax.Precision.HIGHEST, preferred_element_type=jnp.float32)


def tree_offsets(sizes):
    strides = []
    for dim, size in enumerate(sizes):
        step = size // 2
        while step >= 1:
            strides.append((dim, step))
            step //= 2
    offsets = []
    for pos in range(2 ** len(strides)):
        off = [0] * len(sizes)
        for bit, (dim, step) in enumerate(strides):
            if (pos >> bit) & 1:
                off[dim] += step
        offsets.append(off)
    return offsets


def solution(mesh):
    names = tuple(mesh.axis_names)
    n_feat = mesh.shape["feat"]
    n_rows = mesh.shape["rows"]
    n_x = n_feat // CORES
    n_y = n_rows // ZLEN

    def lin(f, r):
        if names[0] == "feat":
            return f * n_rows + r
        return r * n_feat + f

    def dev(x, c, y, z):
        return lin((x % n_x) * CORES + (c % CORES), (y % n_y) * ZLEN + (z % ZLEN))

    def tree(value, me, groups):
        roots = jnp.array([g[0] for g in groups], jnp.int32)
        held = jnp.where(jnp.any(roots == me), value, jnp.zeros_like(value))
        step = 1
        while step < len(groups[0]):
            pairs = [(g[i], g[i + step]) for g in groups for i in range(step)]
            held = held + lax.ppermute(held, names, pairs)
            step *= 2
        return held

    feat_offsets = tree_offsets([n_x, CORES])
    all_offsets = tree_offsets([n_y, ZLEN, n_x, CORES])

    def whole_tree(root_r):
        y0, z0 = divmod(root_r, ZLEN)
        return [[dev(o[2], o[3], y0 + o[0], z0 + o[1]) for o in all_offsets]]

    def per_device(kernel, train_feats, test_feats):
        blk_rows, blk_cols = kernel.shape
        span = NPAN * PANEL
        row_index = lax.axis_index("rows")
        feat_index = lax.axis_index("feat")
        me = lin(feat_index, row_index)
        row_ids = row_index * blk_rows + jnp.arange(blk_rows, dtype=jnp.int32)
        col_ids = feat_index * blk_cols + jnp.arange(blk_cols, dtype=jnp.int32)
        identity = jnp.eye(PANEL, dtype=jnp.float32)

        own = jnp.concatenate([kernel[:, :span], train_feats[:, :span], test_feats[:, :span]], axis=0)
        feat_groups = [[lin(o[0] * CORES + o[1], r) for o in feat_offsets] for r in range(n_rows)]
        own = tree(own, me, feat_groups)

        diag0 = tree(kernel[:, :PANEL], me, whole_tree(0))
        diag1 = tree(kernel[:, :span], me, whole_tree(1))
        diag1, kernel, train_feats, test_feats = lax.optimization_barrier(
            (diag1, kernel, train_feats, test_feats))

        group = blk_cols // blk_rows
        pieces = n_rows // group
        piece_rows = blk_rows // pieces
        stacked = jnp.stack([kernel[:, :span], test_feats[:, :span]])
        piece = None
        for j in range(pieces):
            pairs = [(lin(0, r), lin(r // group, (r % group) * pieces + j)) for r in range(n_rows)]
            got = lax.ppermute(stacked[:, j * piece_rows:(j + 1) * piece_rows], names, pairs)
            piece = got if piece is None else piece + got
        column = lax.all_gather(piece, "rows", axis=1, tiled=True)

        factor0 = jnp.linalg.cholesky(diag0)
        first = jax.scipy.linalg.solve_triangular(factor0, identity, lower=True).T
        cross = product(diag1[:, :PANEL], first)
        factor1 = jnp.linalg.cholesky(diag1[:, PANEL:] - product(cross, cross.T))
        second = jax.scipy.linalg.solve_triangular(factor1, identity, lower=True).T

        def coords(block, ids=None):
            c0 = bulk_product(block[:, :PANEL], first)
            c1 = bulk_product(block[:, PANEL:] - bulk_product(c0, cross.T), second)
            if ids is not None:
                c1 = jnp.where((ids >= PANEL)[:, None], c1, 0.0)
            return jnp.concatenate([c0, c1], axis=1)

        left_rows = coords(own[:blk_rows], row_ids)
        train_rows = coords(own[blk_rows:blk_rows + train_feats.shape[0]])
        test_rows = coords(own[blk_rows + train_feats.shape[0]:])
        right_rows = coords(column[0], col_ids)
        test_cols = coords(column[1])

        in_panel = (col_ids < span)[None, :]
        pad = ((0, 0), (0, blk_cols - span))

        def finish(state, rows):
            updated = state - bulk_product(rows, right_rows.T)
            return jnp.where(in_panel, jnp.pad(rows, pad), updated)

        matrix = finish(kernel, left_rows)
        upper = (row_ids[:, None] < span) & (col_ids[None, :] >= span)
        matrix = jnp.where(upper, 0.0, matrix)
        train_work = finish(train_feats, train_rows)
        test_work = finish(test_feats, test_rows)
        scores = bulk_product(train_rows, test_cols.T)
        return (matrix, train_work, test_work, scores)

    return jax.shard_map(
        per_device,
        mesh=mesh,
        in_specs=(P("rows", "feat"), P("rows", "feat"), P("rows", "feat")),
        out_specs=(P("rows", "feat"), P("rows", "feat"), P("rows", "feat"), P("rows", "feat")),
        check_vma=False,
    )
```

```python
import jax
import jax.numpy as jnp
from jax import lax
from jax.sharding import PartitionSpec as P

PANEL = 256
NPAN = 2
CORES = 2
ZLEN = 8


def product(left, right):
    return jnp.dot(left, right, precision=lax.Precision.HIGHEST, preferred_element_type=jnp.float32)


def bulk_product(left, right):
    return jnp.dot(left, right, precision=lax.Precision.HIGHEST, preferred_element_type=jnp.float32)


def tree_offsets(sizes):
    strides = []
    for dim, size in enumerate(sizes):
        step = size // 2
        while step >= 1:
            strides.append((dim, step))
            step //= 2
    offsets = []
    for pos in range(2 ** len(strides)):
        off = [0] * len(sizes)
        for bit, (dim, step) in enumerate(strides):
            if (pos >> bit) & 1:
                off[dim] += step
        offsets.append(off)
    return offsets


def solution(mesh):
    names = tuple(mesh.axis_names)
    n_feat = mesh.shape["feat"]
    n_rows = mesh.shape["rows"]
    n_x = n_feat // CORES
    n_y = n_rows // ZLEN

    def lin(f, r):
        if names[0] == "feat":
            return f * n_rows + r
        return r * n_feat + f

    def dev(x, c, y, z):
        return lin((x % n_x) * CORES + (c % CORES), (y % n_y) * ZLEN + (z % ZLEN))

    def tree(value, me, groups):
        roots = jnp.array([g[0] for g in groups], jnp.int32)
        held = jnp.where(jnp.any(roots == me), value, jnp.zeros_like(value))
        step = 1
        while step < len(groups[0]):
            pairs = [(g[i], g[i + step]) for g in groups for i in range(step)]
            held = held + lax.ppermute(held, names, pairs)
            step *= 2
        return held

    feat_offsets = tree_offsets([n_x, CORES])
    all_offsets = tree_offsets([n_y, ZLEN, n_x, CORES])

    def whole_tree(root_r):
        y0, z0 = divmod(root_r, ZLEN)
        return [[dev(o[2], o[3], y0 + o[0], z0 + o[1]) for o in all_offsets]]

    def per_device(kernel, train_feats, test_feats):
        blk_rows, blk_cols = kernel.shape
        span = NPAN * PANEL
        row_index = lax.axis_index("rows")
        feat_index = lax.axis_index("feat")
        me = lin(feat_index, row_index)
        row_ids = row_index * blk_rows + jnp.arange(blk_rows, dtype=jnp.int32)
        col_ids = feat_index * blk_cols + jnp.arange(blk_cols, dtype=jnp.int32)
        identity = jnp.eye(PANEL, dtype=jnp.float32)

        own = jnp.concatenate([kernel[:, :span], train_feats[:, :span], test_feats[:, :span]], axis=0)
        feat_groups = [[lin(o[0] * CORES + o[1], r) for o in feat_offsets] for r in range(n_rows)]
        own = tree(own, me, feat_groups)

        diag0 = tree(kernel[:, :PANEL], me, whole_tree(0))
        diag1 = tree(kernel[:, :span], me, whole_tree(1))
        diag0, diag1, kernel, train_feats, test_feats = lax.optimization_barrier(
            (diag0, diag1, kernel, train_feats, test_feats))

        group = blk_cols // blk_rows
        pieces = n_rows // group
        piece_rows = blk_rows // pieces
        stacked = jnp.stack([kernel[:, :span], test_feats[:, :span]])
        piece = None
        for j in range(pieces):
            pairs = [(lin(0, r), lin(r // group, (r % group) * pieces + j)) for r in range(n_rows)]
            got = lax.ppermute(stacked[:, j * piece_rows:(j + 1) * piece_rows], names, pairs)
            piece = got if piece is None else piece + got
        column = lax.all_gather(piece, "rows", axis=1, tiled=True)

        factor0 = jnp.linalg.cholesky(diag0)
        first = jax.scipy.linalg.solve_triangular(factor0, identity, lower=True).T
        cross = product(diag1[:, :PANEL], first)
        factor1 = jnp.linalg.cholesky(diag1[:, PANEL:] - product(cross, cross.T))
        second = jax.scipy.linalg.solve_triangular(factor1, identity, lower=True).T

        def coords(block, ids=None):
            c0 = bulk_product(block[:, :PANEL], first)
            c1 = bulk_product(block[:, PANEL:] - bulk_product(c0, cross.T), second)
            if ids is not None:
                c1 = jnp.where((ids >= PANEL)[:, None], c1, 0.0)
            return jnp.concatenate([c0, c1], axis=1)

        n_own, n_col = own.shape[0], column.shape[1]
        free = jnp.full((n_own - blk_rows,), span, jnp.int32)
        ids = jnp.concatenate([row_ids, free, col_ids, jnp.full((n_col,), span, jnp.int32)])
        every = coords(jnp.concatenate([own, column[0], column[1]], axis=0), ids)
        left_rows = every[:blk_rows]
        train_rows = every[blk_rows:blk_rows + train_feats.shape[0]]
        test_rows = every[blk_rows + train_feats.shape[0]:n_own]
        right_rows = every[n_own:n_own + n_col]
        test_cols = every[n_own + n_col:]

        in_panel = (col_ids < span)[None, :]
        pad = ((0, 0), (0, blk_cols - span))

        def finish(state, rows):
            updated = state - bulk_product(rows, right_rows.T)
            return jnp.where(in_panel, jnp.pad(rows, pad), updated)

        matrix = finish(kernel, left_rows)
        upper = (row_ids[:, None] < span) & (col_ids[None, :] >= span)
        matrix = jnp.where(upper, 0.0, matrix)
        train_work = finish(train_feats, train_rows)
        test_work = finish(test_feats, test_rows)
        scores = bulk_product(train_rows, test_cols.T)
        return (matrix, train_work, test_work, scores)

    return jax.shard_map(
        per_device,
        mesh=mesh,
        in_specs=(P("rows", "feat"), P("rows", "feat"), P("rows", "feat")),
        out_specs=(P("rows", "feat"), P("rows", "feat"), P("rows", "feat"), P("rows", "feat")),
        check_vma=False,
    )
```

```python
import jax
import jax.numpy as jnp
from jax import lax
from jax.sharding import PartitionSpec as P

PANEL = 256
NPAN = 2
CORES = 2
ZLEN = 8


def product(left, right):
    return jnp.dot(left, right, precision=lax.Precision.HIGHEST, preferred_element_type=jnp.float32)


def bulk_product(left, right):
    return jnp.dot(left, right, precision=lax.Precision.HIGHEST, preferred_element_type=jnp.float32)


def tree_offsets(sizes):
    strides = []
    for dim, size in enumerate(sizes):
        step = size // 2
        while step >= 1:
            strides.append((dim, step))
            step //= 2
    offsets = []
    for pos in range(2 ** len(strides)):
        off = [0] * len(sizes)
        for bit, (dim, step) in enumerate(strides):
            if (pos >> bit) & 1:
                off[dim] += step
        offsets.append(off)
    return offsets


def solution(mesh):
    names = tuple(mesh.axis_names)
    n_feat = mesh.shape["feat"]
    n_rows = mesh.shape["rows"]
    n_x = n_feat // CORES
    n_y = n_rows // ZLEN

    def lin(f, r):
        if names[0] == "feat":
            return f * n_rows + r
        return r * n_feat + f

    def dev(x, c, y, z):
        return lin((x % n_x) * CORES + (c % CORES), (y % n_y) * ZLEN + (z % ZLEN))

    def tree(value, me, groups):
        roots = jnp.array([g[0] for g in groups], jnp.int32)
        held = jnp.where(jnp.any(roots == me), value, jnp.zeros_like(value))
        step = 1
        while step < len(groups[0]):
            pairs = [(g[i], g[i + step]) for g in groups for i in range(step)]
            held = held + lax.ppermute(held, names, pairs)
            step *= 2
        return held

    feat_offsets = tree_offsets([n_x, CORES])
    all_offsets = tree_offsets([ZLEN, n_y, n_x, CORES])

    def whole_tree(root_r):
        y0, z0 = divmod(root_r, ZLEN)
        return [[dev(o[2], o[3], y0 + o[1], z0 + o[0]) for o in all_offsets]]

    def per_device(kernel, train_feats, test_feats):
        blk_rows, blk_cols = kernel.shape
        span = NPAN * PANEL
        row_index = lax.axis_index("rows")
        feat_index = lax.axis_index("feat")
        me = lin(feat_index, row_index)
        row_ids = row_index * blk_rows + jnp.arange(blk_rows, dtype=jnp.int32)
        col_ids = feat_index * blk_cols + jnp.arange(blk_cols, dtype=jnp.int32)
        identity = jnp.eye(PANEL, dtype=jnp.float32)

        own = jnp.concatenate([kernel[:, :span], train_feats[:, :span], test_feats[:, :span]], axis=0)
        feat_groups = [[lin(o[0] * CORES + o[1], r) for o in feat_offsets] for r in range(n_rows)]
        own = tree(own, me, feat_groups)

        diag0 = tree(kernel[:, :PANEL], me, whole_tree(0))
        diag1 = tree(kernel[:, :span], me, whole_tree(1))
        diag0, diag1, kernel, train_feats, test_feats = lax.optimization_barrier(
            (diag0, diag1, kernel, train_feats, test_feats))

        group = blk_cols // blk_rows
        pieces = n_rows // group
        piece_rows = blk_rows // pieces
        stacked = jnp.stack([kernel[:, :span], test_feats[:, :span]])
        piece = None
        for j in range(pieces):
            pairs = [(lin(0, r), lin(r // group, (r % group) * pieces + j)) for r in range(n_rows)]
            got = lax.ppermute(stacked[:, j * piece_rows:(j + 1) * piece_rows], names, pairs)
            piece = got if piece is None else piece + got
        column = lax.all_gather(piece, "rows", axis=1, tiled=True)

        factor0 = jnp.linalg.cholesky(diag0)
        first = jax.scipy.linalg.solve_triangular(factor0, identity, lower=True).T
        cross = product(diag1[:, :PANEL], first)
        factor1 = jnp.linalg.cholesky(diag1[:, PANEL:] - product(cross, cross.T))
        second = jax.scipy.linalg.solve_triangular(factor1, identity, lower=True).T

        def coords(block, ids=None):
            c0 = bulk_product(block[:, :PANEL], first)
            c1 = bulk_product(block[:, PANEL:] - bulk_product(c0, cross.T), second)
            if ids is not None:
                c1 = jnp.where((ids >= PANEL)[:, None], c1, 0.0)
            return jnp.concatenate([c0, c1], axis=1)

        left_rows = coords(own[:blk_rows], row_ids)
        train_rows = coords(own[blk_rows:blk_rows + train_feats.shape[0]])
        test_rows = coords(own[blk_rows + train_feats.shape[0]:])
        right_rows = coords(column[0], col_ids)
        test_cols = coords(column[1])

        in_panel = (col_ids < span)[None, :]
        pad = ((0, 0), (0, blk_cols - span))

        def finish(state, rows):
            updated = state - bulk_product(rows, right_rows.T)
            return jnp.where(in_panel, jnp.pad(rows, pad), updated)

        matrix = finish(kernel, left_rows)
        upper = (row_ids[:, None] < span) & (col_ids[None, :] >= span)
        matrix = jnp.where(upper, 0.0, matrix)
        train_work = finish(train_feats, train_rows)
        test_work = finish(test_feats, test_rows)
        scores = bulk_product(train_rows, test_cols.T)
        return (matrix, train_work, test_work, scores)

    return jax.shard_map(
        per_device,
        mesh=mesh,
        in_specs=(P("rows", "feat"), P("rows", "feat"), P("rows", "feat")),
        out_specs=(P("rows", "feat"), P("rows", "feat"), P("rows", "feat"), P("rows", "feat")),
        check_vma=False,
    )
```
